512 devices in a mesh: lat: 16 (over y_hi, x, core), lon: 32 (over z, y_lo).
Axes of the slice: x: 4, y: 8 (y_hi: 2, y_lo: 4; y = y_hi * 4 + y_lo), z: 8, core: 2. Of those that a mesh axis runs over, the one named last changes fastest.
Arguments:
- queries: bfloat16 [131072, 1024], P(('lat', 'lon')), may hold values from -6 to 6
- gain: bfloat16 [1024], replicated, may hold values from 0.099609375 to 1.8984375
- w_query: bfloat16 [1024, 1024], P('lon'), may hold values from -0.1875 to 0.1875
- w_out: bfloat16 [1024, 1024], P(None, 'lon'), may hold values from -0.75 to 0.75
- kv_cache: bfloat16 [2, 32, 256, 1024], P(None, 'lat'), may hold values from -60 to 60
- nbr_lists: int32 [512, 4], P(('lat', 'lon')), may hold values from 0 to 31, as said below
- counts: int32 [512], P(('lat', 'lon')), may hold values from 1 to 4, as said below
Outputs:
- decoded: bfloat16 [131072, 1024], P(('lat', 'lon'))
The draws below stay inside these ranges and needn't reach their ends.
Inputs may be any that keep to these rules, and one draw needn't show every extreme that they name: `nbr_lists`: query block b lies in band b // 32; band k holds latent blocks k * 2 to (k+1) * 2 - 1. Entries of b's list lie in its band or the bands beside it; its first counts[b] entries differ, the others repeat entry 0. `counts`: query blocks of the first and last band have 4 valid slots.
All inputs are finite; a program needn't handle non-finite values.
Results may differ from the reference program's by a relative error of at most 0.007.
The reference program's roundings to bfloat16 on the way count: a program that leaves them out, or rounds other values in their place, can miss the bound.
Values may be sent and summed in bfloat16 or wider, within the bound.
No kernel may reach another device: no remote copies, remote signals or barrier semaphores. Data moves between devices by JAX's collectives and lax.ppermute only.
A program may use at most 64 MiB of HBM per device.

```python
import jax
import jax.numpy as jnp
from jax import lax

MODEL_WIDTH = 1024
H = 16
HD = 64
BLOCK_TOKENS = 256
NBR = 4
BLK_DEV = 2
QB_DEV = 1
NQB = 512
TOKENS = 131072
LATENT_BLOCKS = 32
N_LAT = 16
N_LON = 32


def neighbour_tables(key):
    list_key, count_key = jax.random.split(jax.random.fold_in(key, 7))
    query_ids = jnp.arange(NQB, dtype=jnp.int32)
    band_of = query_ids // (QB_DEV * N_LON)
    lower = jnp.maximum(band_of - 1, 0)
    upper = jnp.minimum(band_of + 1, N_LAT - 1)
    span_blocks = (upper - lower + 1) * BLK_DEV
    positions = jnp.arange(3 * BLK_DEV, dtype=jnp.int32)
    ranking = jax.random.randint(list_key, (NQB, 3 * BLK_DEV), 0, 2 ** 20, dtype=jnp.int32) * 64 + positions[None, :]
    ranking = jnp.where(positions[None, :] < span_blocks[:, None], ranking, 2 ** 30)
    picked = jnp.argsort(ranking, axis=1, stable=True)[:, :NBR].astype(jnp.int32)
    polar = (band_of == 0) | (band_of == N_LAT - 1)
    drawn_counts = jax.random.randint(count_key, (NQB,), 1, NBR + 1, dtype=jnp.int32)
    valid_counts = jnp.where(polar, NBR, drawn_counts).astype(jnp.int32)
    entries = lower[:, None] * BLK_DEV + picked
    slot_ids = jnp.arange(NBR, dtype=jnp.int32)
    entries = jnp.where(slot_ids[None, :] < valid_counts[:, None], entries, entries[:, :1])
    return (entries.astype(jnp.int32), valid_counts)


def draw_nbr_lists(key, part):
    return neighbour_tables(key)[0]


def draw_counts(key, part):
    return neighbour_tables(key)[1]


def draw_kv_cache(key, part):
    key_part, value_part = jax.random.split(jax.random.fold_in(key, 11), 2)
    array_shape = (LATENT_BLOCKS, BLOCK_TOKENS, MODEL_WIDTH)
    key_data = 1.5 * jax.random.truncated_normal(key_part, -4.0, 4.0, array_shape, jnp.float32)
    value_data = jax.random.truncated_normal(value_part, -4.0, 4.0, array_shape, jnp.float32)
    return jnp.stack([key_data, value_data]).astype(jnp.bfloat16)


def steps_of(stream_key, dims, pieces, least, high):
    def one(axis_at, shards_of):
        steps = jax.random.uniform(jax.random.fold_in(jax.random.fold_in(stream_key, 6), axis_at), (shards_of,), jnp.float32, least / len(pieces), high / len(pieces))
        return jnp.repeat(jnp.exp(steps), dims[axis_at] // shards_of).reshape((-1,) + (1,) * (len(dims) - axis_at - 1))

    level = one(*pieces[0])
    for cut in pieces[1:]:
        level = level * one(*cut)
    return level


def gaussian(key, dims, scale, most, cuts=(), held_as=jnp.bfloat16):
    drawn = scale * jax.random.normal(key, dims, jnp.float32)
    if cuts:
        drawn = drawn * steps_of(key, dims, cuts, -0.22, 0.18)
    return jnp.clip(drawn, -most, most).astype(held_as)


def setup_inputs(seed: int = 0) -> dict:
    key_list = jax.random.split(jax.random.key(seed), 8)
    queries = gaussian(key_list[0], (TOKENS, MODEL_WIDTH), 1.0, 6.0, ((0, 512),))
    gain = jnp.clip(1.0 + 0.18 * jax.random.normal(key_list[1], (MODEL_WIDTH,), jnp.float32), 0.099609375, 1.8984375).astype(jnp.bfloat16)
    w_query = gaussian(key_list[2], (MODEL_WIDTH, MODEL_WIDTH), MODEL_WIDTH ** -0.5, 0.1875, ((0, 32),))
    w_out = gaussian(key_list[3], (MODEL_WIDTH, MODEL_WIDTH), (MODEL_WIDTH // 16) ** -0.5, 0.75, ((1, 32),))
    kv_cache = draw_kv_cache(jax.random.fold_in(key_list[7], 71), 0)
    nbr_lists = draw_nbr_lists(jax.random.fold_in(key_list[7], 71), 0)
    counts = draw_counts(jax.random.fold_in(key_list[7], 71), 0)
    return dict(queries=queries, gain=gain, w_query=w_query, w_out=w_out, kv_cache=kv_cache, nbr_lists=nbr_lists, counts=counts)


def reference(queries, gain, w_query, w_out, kv_cache, nbr_lists, counts):
    rows = queries.astype(jnp.float32)
    rowwise_scale = lax.rsqrt(lax.optimization_barrier(jnp.mean(rows * rows, axis=1, keepdims=True)) + 1e-05)
    normed = (rows * rowwise_scale * gain.astype(jnp.float32)[None, :]).astype(jnp.bfloat16)
    query = (jnp.dot(normed, w_query, preferred_element_type=jnp.float32) * HD ** (-0.5)).astype(jnp.bfloat16)
    query_blocks = query.reshape(NQB, BLOCK_TOKENS, H, HD)
    slot_ids = jnp.arange(NBR, dtype=jnp.int32)

    def attend(inputs):
        q_block, listed, count_one = inputs
        key_rows = jnp.take(kv_cache[0], listed, axis=0).reshape(NBR * BLOCK_TOKENS, H, HD).astype(jnp.float32)
        value_rows = jnp.take(kv_cache[1], listed, axis=0).reshape(NBR * BLOCK_TOKENS, H, HD).astype(jnp.float32)
        scores = jnp.einsum('qhd,khd->qhk', q_block.astype(jnp.float32), key_rows)
        live_keys = jnp.repeat(slot_ids < count_one, BLOCK_TOKENS)
        scores = jnp.where(live_keys[None, None, :], scores, -jnp.inf)
        peak = lax.optimization_barrier(jnp.max(scores, axis=2, keepdims=True))
        expo = jnp.exp(scores - peak)
        total = lax.optimization_barrier(jnp.sum(expo, axis=2, keepdims=True))
        rounded = lax.optimization_barrier(expo.astype(jnp.bfloat16)).astype(jnp.float32)
        mixed = jnp.einsum('qhk,khd->qhd', rounded, value_rows)
        return (mixed / total).astype(jnp.bfloat16)
    attended = lax.map(attend, (query_blocks, nbr_lists, counts)).reshape(TOKENS, MODEL_WIDTH)
    return jnp.dot(attended, w_out, preferred_element_type=jnp.float32).astype(jnp.bfloat16)
```

```python
import jax
import jax.numpy as jnp
from jax import lax
from jax.sharding import PartitionSpec as P

H = 16
HD = 64
BLOCK_TOKENS = 256


def padded(array, sides, width):
    for axis, dim in sides:
        devices, length = (lax.axis_size(axis), array.shape[dim])
        up = [(i, (i + 1) % devices) for i in range(devices - 1)]
        down = [(j, i) for i, j in up]
        last = lax.slice_in_dim(array, length - width, length, axis=dim)
        initial = lax.slice_in_dim(array, 0, width, axis=dim)
        before = lax.ppermute(last, axis, up)
        after = lax.ppermute(initial, axis, down)
        array = jnp.concatenate([before, array, after], axis=dim)
    return array


def gathered_rows(local):
    lon_count = lax.axis_size("lon")
    core = lax.axis_index("lat") % 2
    half = local.shape[1] // 2
    mine = lax.dynamic_slice_in_dim(local, core * half, half, axis=1)
    fetched = lax.all_to_all(jnp.tile(mine, (lon_count, 1)), "lon", 0, 0, tiled=True)
    lat_count = lax.axis_size("lat")
    swap = [(i, i ^ 1) for i in range(lat_count)]
    other = lax.ppermute(fetched, "lat", swap)
    low = jnp.where(core == 0, fetched, other)
    high = jnp.where(core == 0, other, fetched)
    return jnp.concatenate([low, high], axis=1)


def on_device(queries, gain, w_query, w_out, kv_cache, nbr_lists, counts):
    rows = queries.astype(jnp.float32)
    rowwise_scale = lax.rsqrt(jnp.mean(rows * rows, axis=1, keepdims=True) + 1e-05)
    normed = (rows * rowwise_scale * gain.astype(jnp.float32)[None, :]).astype(jnp.bfloat16)
    row_count = queries.shape[0]
    query_count = row_count // BLOCK_TOKENS
    projected = jnp.dot(
        normed,
        gathered_rows(w_query),
        preferred_element_type=jnp.float32,
    )
    query = (projected * HD ** (-0.5)).astype(jnp.bfloat16)
    q_heads = query.reshape(query_count, BLOCK_TOKENS, H, HD)
    lat_index = lax.axis_index("lat")
    blocks_here = kv_cache.shape[1]
    window = padded(kv_cache, (("lat", 1),), blocks_here)
    key_window = window[0].reshape(3 * blocks_here, BLOCK_TOKENS, H, HD)
    value_window = window[1].reshape(3 * blocks_here, BLOCK_TOKENS, H, HD)
    local_lists = nbr_lists - (lat_index - 1) * blocks_here

    def update(state, scores, is_live, value_rows, value_form):
        best, total_sum, running = state
        peak = jnp.max(scores, axis=3)
        new_best = jnp.where(is_live[:, None, None], jnp.maximum(best, peak), best)
        rescale = jnp.exp(best - new_best)
        expo = jnp.where(is_live[:, None, None, None], jnp.exp(scores - new_best[..., None]), 0.0)
        total_sum = total_sum * rescale + jnp.sum(expo, axis=3)
        mixed = jnp.einsum(
            value_form, expo.astype(jnp.bfloat16), value_rows, preferred_element_type=jnp.float32
        )
        running = running * rescale[..., None] + mixed
        return (new_best, total_sum, running)

    start_state = (
        jnp.full((query_count, BLOCK_TOKENS, H), -1e30, jnp.float32),
        jnp.zeros((query_count, BLOCK_TOKENS, H), jnp.float32),
        jnp.zeros((query_count, BLOCK_TOKENS, H, HD), jnp.float32),
    )

    def listed_step(slot_index, state):
        picked = lax.dynamic_slice_in_dim(local_lists, slot_index, 1, 1)[:, 0]
        key_rows = jnp.take(key_window, picked, axis=0)
        value_rows = jnp.take(value_window, picked, axis=0)
        scores = jnp.einsum(
            "bqhd,bkhd->bqhk", q_heads, key_rows, preferred_element_type=jnp.float32
        )
        return update(state, scores, slot_index < counts, value_rows, "bqhk,bkhd->bqhd")

    final_state = lax.fori_loop(0, jnp.max(counts), listed_step, start_state)
    attended = (
        (final_state[2] / final_state[1][..., None]).reshape(row_count, H * HD).astype(jnp.bfloat16)
    )
    decoded = lax.dot_general(
        attended,
        gathered_rows(w_out.T),
        (((1,), (1,)), ((), ())),
        preferred_element_type=jnp.float32,
    )
    return decoded.astype(jnp.bfloat16)


def solution(mesh):
    placed = (
        P(("lat", "lon"), None),
        P(),
        P("lon", None),
        P(None, "lon"),
        P(None, "lat", None, None),
        P(("lat", "lon"), None),
        P(("lat", "lon")),
    )
    return jax.shard_map(
        on_device, mesh=mesh, in_specs=placed, out_specs=P(("lat", "lon"), None), check_vma=False
    )
```

```python
import jax
import jax.numpy as jnp
from jax import lax
from jax.experimental import pallas as pl
from jax.experimental.pallas import tpu as pltpu
from jax.sharding import PartitionSpec as P

H = 16
HD = 64
BLOCK_TOKENS = 256


def attention_kernel(slots_ref, count_ref, q_ref, *refs):
    key_refs, value_refs, out_ref = refs[: (len(refs) - 1) // 2], refs[(len(refs) - 1) // 2 : -1], refs[-1]
    count = count_ref[0]
    width = q_ref.shape[1]
    lane = lax.broadcasted_iota(jnp.int32, (1, width), 1)
    q_all = q_ref[...]
    result = None
    for head in range(width // HD):
        in_head = (lane >= head * HD) & (lane < (head + 1) * HD)
        q_head = jnp.where(in_head, q_all, jnp.zeros_like(q_all))
        scores = []
        for slot, key_ref in enumerate(key_refs):
            s = lax.dot_general(q_head, key_ref[...], (((1,), (1,)), ((), ())), preferred_element_type=jnp.float32)
            scores.append(jnp.where(slot < count, s, -jnp.inf))
        peak = scores[0].max(axis=1, keepdims=True)
        for s in scores[1:]:
            peak = jnp.maximum(peak, s.max(axis=1, keepdims=True))
        total = None
        mixed = None
        for s, value_ref in zip(scores, value_refs):
            expo = jnp.exp(s - peak)
            part = expo.sum(axis=1, keepdims=True)
            total = part if total is None else total + part
            term = jnp.dot(expo.astype(jnp.bfloat16), value_ref[...], preferred_element_type=jnp.float32)
            mixed = term if mixed is None else mixed + term
        head_out = mixed / total
        result = head_out if result is None else jnp.where(in_head, head_out, result)
    out_ref[...] = result.astype(out_ref.dtype)


def attend(q, window, slots, count, lanes=128):
    rows, width = q.shape
    nbr = slots.shape[0]
    q_spec = pl.BlockSpec((rows, lanes), lambda h, s, c: (0, h))
    def kv_spec(part, slot):
        return pl.BlockSpec((None, None, rows, lanes), lambda h, s, c: (part, s[slot], 0, h))
    in_specs = [q_spec] + [kv_spec(0, j) for j in range(nbr)] + [kv_spec(1, j) for j in range(nbr)]
    return pl.pallas_call(
        attention_kernel,
        grid_spec=pltpu.PrefetchScalarGridSpec(
            num_scalar_prefetch=2, grid=(width // lanes,), in_specs=in_specs, out_specs=q_spec),
        out_shape=jax.ShapeDtypeStruct((rows, width), jnp.bfloat16),
    )(slots, count, q, *([window] * (2 * nbr)))


def padded(array, sides, width):
    for axis, dim in sides:
        devices, length = (lax.axis_size(axis), array.shape[dim])
        up = [(i, (i + 1) % devices) for i in range(devices - 1)]
        down = [(j, i) for i, j in up]
        last = lax.slice_in_dim(array, length - width, length, axis=dim)
        initial = lax.slice_in_dim(array, 0, width, axis=dim)
        before = lax.ppermute(last, axis, up)
        after = lax.ppermute(initial, axis, down)
        array = jnp.concatenate([before, array, after], axis=dim)
    return array


def gathered_rows(local):
    lon_count = lax.axis_size("lon")
    core = lax.axis_index("lat") % 2
    half = local.shape[1] // 2
    mine = lax.dynamic_slice_in_dim(local, core * half, half, axis=1)
    fetched = lax.all_to_all(jnp.tile(mine, (lon_count, 1)), "lon", 0, 0, tiled=True)
    lat_count = lax.axis_size("lat")
    swap = [(i, i ^ 1) for i in range(lat_count)]
    other = lax.ppermute(fetched, "lat", swap)
    low = jnp.where(core == 0, fetched, other)
    high = jnp.where(core == 0, other, fetched)
    return jnp.concatenate([low, high], axis=1)


def on_device(queries, gain, w_query, w_out, kv_cache, nbr_lists, counts):
    rows = queries.astype(jnp.float32)
    rowwise_scale = lax.rsqrt(jnp.mean(rows * rows, axis=1, keepdims=True) + 1e-05)
    normed = (rows * rowwise_scale * gain.astype(jnp.float32)[None, :]).astype(jnp.bfloat16)
    projected = jnp.dot(
        normed,
        gathered_rows(w_query),
        preferred_element_type=jnp.float32,
    )
    query = (projected * HD ** (-0.5)).astype(jnp.bfloat16)
    blocks_here = kv_cache.shape[1]
    window = padded(kv_cache, (("lat", 1),), blocks_here)
    local_lists = nbr_lists - (lax.axis_index("lat") - 1) * blocks_here
    slots = jnp.clip(local_lists[0], 0, window.shape[1] - 1)
    attended = attend(query, window, slots, counts)
    decoded = lax.dot_general(
        attended,
        gathered_rows(w_out.T),
        (((1,), (1,)), ((), ())),
        preferred_element_type=jnp.float32,
    )
    return decoded.astype(jnp.bfloat16)


def solution(mesh):
    placed = (
        P(("lat", "lon"), None),
        P(),
        P("lon", None),
        P(None, "lon"),
        P(None, "lat", None, None),
        P(("lat", "lon"), None),
        P(("lat", "lon")),
    )
    return jax.shard_map(
        on_device, mesh=mesh, in_specs=placed, out_specs=P(("lat", "lon"), None), check_vma=False
    )
```

```python
import jax
import jax.numpy as jnp
from jax import lax
from jax.experimental import pallas as pl
from jax.experimental.pallas import tpu as pltpu
from jax.sharding import PartitionSpec as P


HD = 64


def attention_kernel(slots_ref, count_ref, q_ref, *refs):
    key_refs, value_refs, out_ref = refs[: (len(refs) - 1) // 2], refs[(len(refs) - 1) // 2 : -1], refs[-1]
    count = count_ref[0]
    width = q_ref.shape[1]
    lane = lax.broadcasted_iota(jnp.int32, (1, width), 1)
    q_all = q_ref[...]
    result = None
    for head in range(width // HD):
        in_head = (lane >= head * HD) & (lane < (head + 1) * HD)
        q_head = jnp.where(in_head, q_all, jnp.zeros_like(q_all))
        scores = []
        for slot, key_ref in enumerate(key_refs):
            s = lax.dot_general(q_head, key_ref[...], (((1,), (1,)), ((), ())), preferred_element_type=jnp.float32)
            scores.append(jnp.where(slot < count, s, -jnp.inf))
        peak = scores[0].max(axis=1, keepdims=True)
        for s in scores[1:]:
            peak = jnp.maximum(peak, s.max(axis=1, keepdims=True))
        total = None
        mixed = None
        for s, value_ref in zip(scores, value_refs):
            expo = jnp.exp(s - peak)
            part = expo.sum(axis=1, keepdims=True)
            total = part if total is None else total + part
            term = jnp.dot(expo.astype(jnp.bfloat16), value_ref[...], preferred_element_type=jnp.float32)
            mixed = term if mixed is None else mixed + term
        head_out = mixed / total
        result = head_out if result is None else jnp.where(in_head, head_out, result)
    out_ref[...] = result.astype(out_ref.dtype)


def attend(q, window, slots, count, lanes=128):
    rows, width = q.shape
    nbr = slots.shape[0]
    q_spec = pl.BlockSpec((rows, lanes), lambda h, s, c: (0, h))
    def kv_spec(part, slot):
        return pl.BlockSpec((None, None, rows, lanes), lambda h, s, c: (part, s[slot], 0, h))
    in_specs = [q_spec] + [kv_spec(0, j) for j in range(nbr)] + [kv_spec(1, j) for j in range(nbr)]
    return pl.pallas_call(
        attention_kernel,
        grid_spec=pltpu.PrefetchScalarGridSpec(
            num_scalar_prefetch=2, grid=(width // lanes,), in_specs=in_specs, out_specs=q_spec),
        out_shape=jax.ShapeDtypeStruct((rows, width), jnp.bfloat16),
    )(slots, count, q, *([window] * (2 * nbr)))


def padded(array, sides, width):
    for axis, dim in sides:
        devices, length = (lax.axis_size(axis), array.shape[dim])
        up = [(i, (i + 1) % devices) for i in range(devices - 1)]
        down = [(j, i) for i, j in up]
        last = lax.slice_in_dim(array, length - width, length, axis=dim)
        initial = lax.slice_in_dim(array, 0, width, axis=dim)
        before = lax.ppermute(last, axis, up)
        after = lax.ppermute(initial, axis, down)
        array = jnp.concatenate([before, array, after], axis=dim)
    return array


def gathered_rows(local, after=None):
    lon_count = lax.axis_size("lon")
    core = lax.axis_index("lat") % 2
    half = local.shape[1] // 2
    mine = lax.dynamic_slice_in_dim(local, core * half, half, axis=1)
    if after is not None:
        mine, _ = lax.optimization_barrier((mine, after))
    fetched = lax.all_to_all(jnp.tile(mine, (lon_count, 1)), "lon", 0, 0, tiled=True)
    lat_count = lax.axis_size("lat")
    swap = [(i, i ^ 1) for i in range(lat_count)]
    other = lax.ppermute(fetched, "lat", swap)
    low = jnp.where(core == 0, fetched, other)
    high = jnp.where(core == 0, other, fetched)
    return jnp.concatenate([low, high], axis=1)


def layer(queries, gain, w_query, w_out, kv_cache, nbr_lists, counts):
    rows = queries.astype(jnp.float32)
    rowwise_scale = lax.rsqrt(jnp.mean(rows * rows, axis=1, keepdims=True) + 1e-05)
    normed = (rows * rowwise_scale * gain.astype(jnp.float32)[None, :]).astype(jnp.bfloat16)
    projected = jnp.dot(
        normed,
        gathered_rows(w_query),
        preferred_element_type=jnp.float32,
    )
    query = (projected * HD ** (-0.5)).astype(jnp.bfloat16)
    blocks_here = kv_cache.shape[1]
    window = padded(kv_cache, (("lat", 1),), blocks_here)
    local_lists = nbr_lists - (lax.axis_index("lat") - 1) * blocks_here
    slots = jnp.clip(local_lists[0], 0, window.shape[1] - 1)
    attended = attend(query, window, slots, counts)
    w_out_rows = gathered_rows(w_out.T, after=query)
    decoded = lax.dot_general(
        attended,
        w_out_rows,
        (((1,), (1,)), ((), ())),
        preferred_element_type=jnp.float32,
    )
    return decoded.astype(jnp.bfloat16)


def solution(mesh):
    placed = (
        P(("lat", "lon"), None),
        P(),
        P("lon", None),
        P(None, "lon"),
        P(None, "lat", None, None),
        P(("lat", "lon"), None),
        P(("lat", "lon")),
    )
    return jax.shard_map(layer, mesh=mesh, in_specs=placed, out_specs=P(("lat", "lon"), None), check_vma=False)
```

```python
import jax
import jax.numpy as jnp
from jax import lax
from jax.experimental import pallas as pl
from jax.experimental.pallas import tpu as pltpu
from jax.sharding import PartitionSpec as P


HD = 64


def attention_kernel(slots_ref, count_ref, q_ref, *refs):
    key_refs, value_refs, out_ref = refs[: (len(refs) - 1) // 2], refs[(len(refs) - 1) // 2 : -1], refs[-1]
    count = count_ref[0]
    width = q_ref.shape[1]
    lane = lax.broadcasted_iota(jnp.int32, (1, width), 1)
    q_all = q_ref[...]
    result = None
    for head in range(width // HD):
        in_head = (lane >= head * HD) & (lane < (head + 1) * HD)
        q_head = jnp.where(in_head, q_all, jnp.zeros_like(q_all))
        scores = []
        for slot, key_ref in enumerate(key_refs):
            s = lax.dot_general(q_head, key_ref[...], (((1,), (1,)), ((), ())), preferred_element_type=jnp.float32)
            scores.append(jnp.where(slot < count, s, -jnp.inf))
        peak = scores[0].max(axis=1, keepdims=True)
        for s in scores[1:]:
            peak = jnp.maximum(peak, s.max(axis=1, keepdims=True))
        total = None
        mixed = None
        for s, value_ref in zip(scores, value_refs):
            expo = jnp.exp(s - peak)
            part = expo.sum(axis=1, keepdims=True)
            total = part if total is None else total + part
            term = jnp.dot(expo.astype(jnp.bfloat16), value_ref[...], preferred_element_type=jnp.float32)
            mixed = term if mixed is None else mixed + term
        head_out = mixed / total
        result = head_out if result is None else jnp.where(in_head, head_out, result)
    out_ref[...] = result.astype(out_ref.dtype)


def attend(q, window, slots, count, lanes=128):
    rows, width = q.shape
    nbr = slots.shape[0]
    q_spec = pl.BlockSpec((rows, lanes), lambda h, s, c: (0, h))
    def kv_spec(part, slot):
        return pl.BlockSpec((None, None, rows, lanes), lambda h, s, c: (part, s[slot], 0, h))
    in_specs = [q_spec] + [kv_spec(0, j) for j in range(nbr)] + [kv_spec(1, j) for j in range(nbr)]
    return pl.pallas_call(
        attention_kernel,
        grid_spec=pltpu.PrefetchScalarGridSpec(
            num_scalar_prefetch=2, grid=(width // lanes,), in_specs=in_specs, out_specs=q_spec),
        out_shape=jax.ShapeDtypeStruct((rows, width), jnp.bfloat16),
    )(slots, count, q, *([window] * (2 * nbr)))


Y_LO = 4


def neighbour_bands(kv):
    lat_count, lon_count = lax.axis_size("lat"), lax.axis_size("lon")
    lat, lon = lax.axis_index("lat"), lax.axis_index("lon")
    both = ("lat", "lon")
    split = lat_count // 2
    up = [(k * lon_count + l, (k + 1) * lon_count + l) for k in range(lat_count - 1) if k != split - 1 for l in range(lon_count)]
    below = lax.ppermute(kv, both, up)
    above = lax.ppermute(kv, both, [(j, i) for i, j in up])
    rows = kv.shape[2] // Y_LO
    y_lo = lon % Y_LO
    piece = lax.dynamic_slice_in_dim(kv, (Y_LO - 1 - y_lo) * rows, rows, axis=2)
    cross = []
    for l in range(lon_count):
        mirror = l - l % Y_LO + (Y_LO - 1 - l % Y_LO)
        cross.append(((split - 1) * lon_count + l, split * lon_count + mirror))
        cross.append((split * lon_count + l, (split - 1) * lon_count + mirror))
    pieces = [lax.ppermute(piece, both, cross)]
    for shift in range(1, Y_LO):
        ring = []
        for band in (split - 1, split):
            for l in range(lon_count):
                ring.append((band * lon_count + l, band * lon_count + l - l % Y_LO + (l % Y_LO + shift) % Y_LO))
        pieces.append(lax.ppermute(pieces[0], both, ring))
    order = (y_lo - jnp.arange(Y_LO)) % Y_LO
    joined = jnp.take(jnp.stack(pieces), order, axis=0)
    joined = jnp.moveaxis(joined, 0, 2).reshape(kv.shape)
    below = jnp.where(lat == split, joined, below)
    above = jnp.where(lat == split - 1, joined, above)
    return below, above


def gathered_rows(local, after=None):
    lon_count = lax.axis_size("lon")
    core = lax.axis_index("lat") % 2
    half = local.shape[1] // 2
    mine = lax.dynamic_slice_in_dim(local, core * half, half, axis=1)
    if after is not None:
        mine, _ = lax.optimization_barrier((mine, after))
    fetched = lax.all_to_all(jnp.tile(mine, (lon_count, 1)), "lon", 0, 0, tiled=True)
    lat_count = lax.axis_size("lat")
    swap = [(i, i ^ 1) for i in range(lat_count)]
    other = lax.ppermute(fetched, "lat", swap)
    low = jnp.where(core == 0, fetched, other)
    high = jnp.where(core == 0, other, fetched)
    return jnp.concatenate([low, high], axis=1)


def layer(queries, gain, w_query, w_out, kv_cache, nbr_lists, counts):
    rows = queries.astype(jnp.float32)
    rowwise_scale = lax.rsqrt(jnp.mean(rows * rows, axis=1, keepdims=True) + 1e-05)
    normed = (rows * rowwise_scale * gain.astype(jnp.float32)[None, :]).astype(jnp.bfloat16)
    projected = jnp.dot(
        normed,
        gathered_rows(w_query),
        preferred_element_type=jnp.float32,
    )
    query = (projected * HD ** (-0.5)).astype(jnp.bfloat16)
    blocks_here = kv_cache.shape[1]
    below, above = neighbour_bands(kv_cache)
    window = jnp.concatenate([below, kv_cache, above], axis=1)
    local_lists = nbr_lists - (lax.axis_index("lat") - 1) * blocks_here
    slots = jnp.clip(local_lists[0], 0, window.shape[1] - 1)
    attended = attend(query, window, slots, counts)
    w_out_rows = gathered_rows(w_out.T, after=query)
    decoded = lax.dot_general(
        attended,
        w_out_rows,
        (((1,), (1,)), ((), ())),
        preferred_element_type=jnp.float32,
    )
    return decoded.astype(jnp.bfloat16)


def solution(mesh):
    placed = (
        P(("lat", "lon"), None),
        P(),
        P("lon", None),
        P(None, "lon"),
        P(None, "lat", None, None),
        P(("lat", "lon"), None),
        P(("lat", "lon")),
    )
    return jax.shard_map(layer, mesh=mesh, in_specs=placed, out_specs=P(("lat", "lon"), None), check_vma=False)
```

```python
import jax
import jax.numpy as jnp
from jax import lax
from jax.experimental import pallas as pl
from jax.experimental.pallas import tpu as pltpu
from jax.sharding import PartitionSpec as P


HD = 64


def attention_kernel(slots_ref, count_ref, q_ref, *refs):
    key_refs, value_refs, out_ref = refs[: (len(refs) - 1) // 2], refs[(len(refs) - 1) // 2 : -1], refs[-1]
    count = count_ref[0]
    width = q_ref.shape[1]
    lane = lax.broadcasted_iota(jnp.int32, (1, width), 1)
    q_all = q_ref[...]
    result = None
    for head in range(width // HD):
        in_head = (lane >= head * HD) & (lane < (head + 1) * HD)
        q_head = jnp.where(in_head, q_all, jnp.zeros_like(q_all))
        scores = []
        for slot, key_ref in enumerate(key_refs):
            s = lax.dot_general(q_head, key_ref[...], (((1,), (1,)), ((), ())), preferred_element_type=jnp.float32)
            scores.append(jnp.where(slot < count, s, -jnp.inf))
        peak = scores[0].max(axis=1, keepdims=True)
        for s in scores[1:]:
            peak = jnp.maximum(peak, s.max(axis=1, keepdims=True))
        total = None
        mixed = None
        for s, value_ref in zip(scores, value_refs):
            expo = jnp.exp(s - peak)
            part = expo.sum(axis=1, keepdims=True)
            total = part if total is None else total + part
            term = jnp.dot(expo.astype(jnp.bfloat16), value_ref[...], preferred_element_type=jnp.float32)
            mixed = term if mixed is None else mixed + term
        head_out = mixed / total
        result = head_out if result is None else jnp.where(in_head, head_out, result)
    out_ref[...] = result.astype(out_ref.dtype)


def attend(q, window, slots, count, lanes=128):
    rows, width = q.shape
    nbr = slots.shape[0]
    q_spec = pl.BlockSpec((rows, lanes), lambda h, s, c: (0, h))

    def kv_spec(part, slot):
        return pl.BlockSpec((None, None, rows, lanes), lambda h, s, c: (part, s[slot], 0, h))

    in_specs = [q_spec] + [kv_spec(0, j) for j in range(nbr)] + [kv_spec(1, j) for j in range(nbr)]
    return pl.pallas_call(
        attention_kernel,
        grid_spec=pltpu.PrefetchScalarGridSpec(
            num_scalar_prefetch=2, grid=(width // lanes,), in_specs=in_specs, out_specs=q_spec),
        out_shape=jax.ShapeDtypeStruct((rows, width), jnp.bfloat16),
    )(slots, count, q, *([window] * (2 * nbr)))


Y_LO = 4


def neighbour_bands(kv):
    lat_count, lon_count = lax.axis_size("lat"), lax.axis_size("lon")
    lat, lon = lax.axis_index("lat"), lax.axis_index("lon")
    both = ("lat", "lon")
    split = lat_count // 2
    up = [(k * lon_count + l, (k + 1) * lon_count + l) for k in range(lat_count - 1) if k != split - 1 for l in range(lon_count)]
    below = lax.ppermute(kv, both, up)
    above = lax.ppermute(kv, both, [(j, i) for i, j in up])
    rows = kv.shape[2] // Y_LO
    z = lon // Y_LO
    z_count = lon_count // Y_LO
    piece = lax.dynamic_slice_in_dim(kv, (z % Y_LO) * rows, rows, axis=2)
    cross = []
    for l in range(lon_count):
        mirror = l - l % Y_LO + (Y_LO - 1 - l % Y_LO)
        cross.append(((split - 1) * lon_count + l, split * lon_count + mirror))
        cross.append((split * lon_count + l, (split - 1) * lon_count + mirror))
    own = lax.ppermute(piece, both, cross)

    def along_z(value, shift):
        pairs = []
        for band in (split - 1, split):
            for l in range(lon_count):
                target = ((l // Y_LO + shift) % z_count) * Y_LO + l % Y_LO
                pairs.append((band * lon_count + l, band * lon_count + target))
        return lax.ppermute(value, both, pairs)

    half = rows // 2
    opposite = jnp.concatenate(
        [along_z(own[:, :, :half], 2), along_z(own[:, :, half:], -2)], axis=2
    )
    quarters = jnp.stack([own, along_z(own, -1), opposite, along_z(own, 1)])
    order = (jnp.arange(Y_LO) - z) % Y_LO
    joined = jnp.take(quarters, order, axis=0)
    joined = jnp.moveaxis(joined, 0, 2).reshape(kv.shape)
    below = jnp.where(lat == split, joined, below)
    above = jnp.where(lat == split - 1, joined, above)
    return below, above


def gathered_rows(local, after=None):
    lon_count = lax.axis_size("lon")
    core = lax.axis_index("lat") % 2
    half = local.shape[1] // 2
    mine = lax.dynamic_slice_in_dim(local, core * half, half, axis=1)
    if after is not None:
        mine, _ = lax.optimization_barrier((mine, after))
    fetched = lax.all_to_all(jnp.tile(mine, (lon_count, 1)), "lon", 0, 0, tiled=True)
    lat_count = lax.axis_size("lat")
    swap = [(i, i ^ 1) for i in range(lat_count)]
    other = lax.ppermute(fetched, "lat", swap)
    low = jnp.where(core == 0, fetched, other)
    high = jnp.where(core == 0, other, fetched)
    return jnp.concatenate([low, high], axis=1)


def layer(queries, gain, w_query, w_out, kv_cache, nbr_lists, counts):
    rows = queries.astype(jnp.float32)
    rowwise_scale = lax.rsqrt(jnp.mean(rows * rows, axis=1, keepdims=True) + 1e-05)
    normed = (rows * rowwise_scale * gain.astype(jnp.float32)[None, :]).astype(jnp.bfloat16)
    w_query_rows = gathered_rows(w_query)
    projected = jnp.dot(
        normed,
        w_query_rows,
        preferred_element_type=jnp.float32,
    )
    query = (projected * HD ** (-0.5)).astype(jnp.bfloat16)
    blocks_here = kv_cache.shape[1]
    below, above = neighbour_bands(kv_cache)
    window = jnp.concatenate([below, kv_cache, above], axis=1)
    local_lists = nbr_lists - (lax.axis_index("lat") - 1) * blocks_here
    slots = jnp.clip(local_lists[0], 0, window.shape[1] - 1)
    attended = attend(query, window, slots, counts)
    w_out_rows = gathered_rows(w_out.T, after=query)
    decoded = lax.dot_general(
        attended,
        w_out_rows,
        (((1,), (1,)), ((), ())),
        preferred_element_type=jnp.float32,
    )
    return decoded.astype(jnp.bfloat16)


def solution(mesh):
    placed = (
        P(("lat", "lon"), None),
        P(),
        P("lon", None),
        P(None, "lon"),
        P(None, "lat", None, None),
        P(("lat", "lon"), None),
        P(("lat", "lon")),
    )
    return jax.shard_map(layer, mesh=mesh, in_specs=placed, out_specs=P(("lat", "lon"), None), check_vma=False)
```

```python
import jax
import jax.numpy as jnp
from jax import lax
from jax.experimental import pallas as pl
from jax.experimental.pallas import tpu as pltpu
from jax.sharding import PartitionSpec as P


HD = 64


def attention_kernel(slots_ref, count_ref, q_ref, *refs):
    key_refs, value_refs, out_ref = refs[: (len(refs) - 1) // 2], refs[(len(refs) - 1) // 2 : -1], refs[-1]
    count = count_ref[0]
    width = q_ref.shape[1]
    lane = lax.broadcasted_iota(jnp.int32, (1, width), 1)
    q_all = q_ref[...]
    result = None
    for head in range(width // HD):
        in_head = (lane >= head * HD) & (lane < (head + 1) * HD)
        q_head = jnp.where(in_head, q_all, jnp.zeros_like(q_all))
        scores = []
        for slot, key_ref in enumerate(key_refs):
            s = lax.dot_general(q_head, key_ref[...], (((1,), (1,)), ((), ())), preferred_element_type=jnp.float32)
            scores.append(jnp.where(slot < count, s, -jnp.inf))
        peak = scores[0].max(axis=1, keepdims=True)
        for s in scores[1:]:
            peak = jnp.maximum(peak, s.max(axis=1, keepdims=True))
        total = None
        mixed = None
        for s, value_ref in zip(scores, value_refs):
            expo = jnp.exp(s - peak)
            part = expo.sum(axis=1, keepdims=True)
            total = part if total is None else total + part
            term = jnp.dot(expo.astype(jnp.bfloat16), value_ref[...], preferred_element_type=jnp.float32)
            mixed = term if mixed is None else mixed + term
        head_out = mixed / total
        result = head_out if result is None else jnp.where(in_head, head_out, result)
    out_ref[...] = result.astype(out_ref.dtype)


def attend(q, window, slots, count, lanes=128):
    rows, width = q.shape
    nbr = slots.shape[0]
    q_spec = pl.BlockSpec((rows, lanes), lambda h, s, c: (0, h))

    def kv_spec(part, slot):
        return pl.BlockSpec((None, None, rows, lanes), lambda h, s, c: (part, s[slot], 0, h))

    in_specs = [q_spec] + [kv_spec(0, j) for j in range(nbr)] + [kv_spec(1, j) for j in range(nbr)]
    return pl.pallas_call(
        attention_kernel,
        grid_spec=pltpu.PrefetchScalarGridSpec(
            num_scalar_prefetch=2, grid=(width // lanes,), in_specs=in_specs, out_specs=q_spec),
        out_shape=jax.ShapeDtypeStruct((rows, width), jnp.bfloat16),
    )(slots, count, q, *([window] * (2 * nbr)))


Y_LO = 4


def neighbour_bands(kv):
    lat_count, lon_count = lax.axis_size("lat"), lax.axis_size("lon")
    lon = lax.axis_index("lon")
    both = ("lat", "lon")
    split = lat_count // 2
    up = [(k * lon_count + l, (k + 1) * lon_count + l) for k in range(lat_count - 1) if k != split - 1 for l in range(lon_count)]
    below = lax.ppermute(kv, both, up)
    above = lax.ppermute(kv, both, [(j, i) for i, j in up])
    rows = kv.shape[2] // Y_LO
    z = lon // Y_LO
    piece = lax.dynamic_slice_in_dim(kv, (z % Y_LO) * rows, rows, axis=2)
    cross = []
    for l in range(lon_count):
        mirror = l - l % Y_LO + (Y_LO - 1 - l % Y_LO)
        cross.append(((split - 1) * lon_count + l, split * lon_count + mirror))
        cross.append((split * lon_count + l, (split - 1) * lon_count + mirror))
    own = lax.ppermute(piece, both, cross)
    return below, above, own


def far_side(kv, below, above, own):
    lat_count, lon_count = lax.axis_size("lat"), lax.axis_size("lon")
    lat, lon = lax.axis_index("lat"), lax.axis_index("lon")
    both = ("lat", "lon")
    split = lat_count // 2
    rows = kv.shape[2] // Y_LO
    z = lon // Y_LO
    z_count = lon_count // Y_LO

    def along_z(value, shift):
        pairs = []
        for band in (split - 1, split):
            for l in range(lon_count):
                target = ((l // Y_LO + shift) % z_count) * Y_LO + l % Y_LO
                pairs.append((band * lon_count + l, band * lon_count + target))
        return lax.ppermute(value, both, pairs)

    half = rows // 2
    opposite = jnp.concatenate(
        [along_z(own[:, :, :half], 2), along_z(own[:, :, half:], -2)], axis=2
    )
    quarters = jnp.stack([own, along_z(own, -1), opposite, along_z(own, 1)])
    order = (jnp.arange(Y_LO) - z) % Y_LO
    joined = jnp.take(quarters, order, axis=0)
    joined = jnp.moveaxis(joined, 0, 2).reshape(kv.shape)
    below = jnp.where(lat == split, joined, below)
    above = jnp.where(lat == split - 1, joined, above)
    return below, above


def gathered_rows(local, after=None):
    lon_count = lax.axis_size("lon")
    core = lax.axis_index("lat") % 2
    half = local.shape[1] // 2
    mine = lax.dynamic_slice_in_dim(local, core * half, half, axis=1)
    if after is not None:
        mine, _ = lax.optimization_barrier((mine, after))
    fetched = lax.all_to_all(jnp.tile(mine, (lon_count, 1)), "lon", 0, 0, tiled=True)
    lat_count = lax.axis_size("lat")
    swap = [(i, i ^ 1) for i in range(lat_count)]
    other = lax.ppermute(fetched, "lat", swap)
    low = jnp.where(core == 0, fetched, other)
    high = jnp.where(core == 0, other, fetched)
    return jnp.concatenate([low, high], axis=1)


def layer(queries, gain, w_query, w_out, kv_cache, nbr_lists, counts):
    rows = queries.astype(jnp.float32)
    rowwise_scale = lax.rsqrt(jnp.mean(rows * rows, axis=1, keepdims=True) + 1e-05)
    normed = (rows * rowwise_scale * gain.astype(jnp.float32)[None, :]).astype(jnp.bfloat16)
    blocks_here = kv_cache.shape[1]
    sent = neighbour_bands(kv_cache)
    w_query_rows = gathered_rows(w_query, after=sent[2])
    projected = jnp.dot(
        normed,
        w_query_rows,
        preferred_element_type=jnp.float32,
    )
    query = (projected * HD ** (-0.5)).astype(jnp.bfloat16)
    local_lists = nbr_lists - (lax.axis_index("lat") - 1) * blocks_here
    slots = jnp.clip(local_lists[0], 0, 3 * blocks_here - 1)
    below, above = far_side(kv_cache, *sent)
    window = jnp.concatenate([below, kv_cache, above], axis=1)
    attended = attend(query, window, slots, counts)
    w_out_rows = gathered_rows(w_out.T, after=query)
    decoded = lax.dot_general(
        attended,
        w_out_rows,
        (((1,), (1,)), ((), ())),
        preferred_element_type=jnp.float32,
    )
    return decoded.astype(jnp.bfloat16)


def solution(mesh):
    placed = (
        P(("lat", "lon"), None),
        P(),
        P("lon", None),
        P(None, "lon"),
        P(None, "lat", None, None),
        P(("lat", "lon"), None),
        P(("lat", "lon")),
    )
    return jax.shard_map(layer, mesh=mesh, in_specs=placed, out_specs=P(("lat", "lon"), None), check_vma=False)
```

```python
import jax
import jax.numpy as jnp
from jax import lax
from jax.experimental import pallas as pl
from jax.experimental.pallas import tpu as pltpu
from jax.sharding import PartitionSpec as P


HD = 64


def attention_kernel(slots_ref, count_ref, q_ref, *refs):
    key_refs, value_refs, out_ref = refs[: (len(refs) - 1) // 2], refs[(len(refs) - 1) // 2 : -1], refs[-1]
    count = count_ref[0]
    width = q_ref.shape[1]
    lane = lax.broadcasted_iota(jnp.int32, (1, width), 1)
    q_all = q_ref[...]
    result = None
    for head in range(width // HD):
        in_head = (lane >= head * HD) & (lane < (head + 1) * HD)
        q_head = jnp.where(in_head, q_all, jnp.zeros_like(q_all))
        scores = []
        for slot, key_ref in enumerate(key_refs):
            s = lax.dot_general(q_head, key_ref[...], (((1,), (1,)), ((), ())), preferred_element_type=jnp.float32)
            scores.append(s if slot == 0 else jnp.where(slot < count, s, -jnp.inf))
        peak = scores[0].max(axis=1, keepdims=True)
        for s in scores[1:]:
            peak = jnp.maximum(peak, s.max(axis=1, keepdims=True))
        total = None
        mixed = None
        for s, value_ref in zip(scores, value_refs):
            expo = jnp.exp(s - peak)
            part = expo.sum(axis=1, keepdims=True)
            total = part if total is None else total + part
            term = jnp.dot(expo.astype(jnp.bfloat16), value_ref[...], preferred_element_type=jnp.float32)
            mixed = term if mixed is None else mixed + term
        head_out = mixed / total
        result = head_out if result is None else jnp.where(in_head, head_out, result)
    out_ref[...] = result.astype(out_ref.dtype)


def attend(q, window, slots, count, lanes=128):
    rows, width = q.shape
    nbr = slots.shape[0]
    q_spec = pl.BlockSpec((rows, lanes), lambda h, s, c: (0, h))

    def kv_spec(part, slot):
        return pl.BlockSpec((None, None, rows, lanes), lambda h, s, c: (part, s[slot], 0, h))

    in_specs = [q_spec] + [kv_spec(0, j) for j in range(nbr)] + [kv_spec(1, j) for j in range(nbr)]
    return pl.pallas_call(
        attention_kernel,
        grid_spec=pltpu.PrefetchScalarGridSpec(
            num_scalar_prefetch=2, grid=(width // lanes,), in_specs=in_specs, out_specs=q_spec),
        out_shape=jax.ShapeDtypeStruct((rows, width), jnp.bfloat16),
    )(slots, count, q, *([window] * (2 * nbr)))


Y_LO = 4


def neighbour_bands(kv):
    lat_count, lon_count = lax.axis_size("lat"), lax.axis_size("lon")
    lon = lax.axis_index("lon")
    both = ("lat", "lon")
    split = lat_count // 2
    up = [(k * lon_count + l, (k + 1) * lon_count + l) for k in range(lat_count - 1) if k != split - 1 for l in range(lon_count)]
    below = lax.ppermute(kv, both, up)
    above = lax.ppermute(kv, both, [(j, i) for i, j in up])
    rows = kv.shape[2] // Y_LO
    z = lon // Y_LO
    piece = lax.dynamic_slice_in_dim(kv, (z % Y_LO) * rows, rows, axis=2)
    cross = []
    for l in range(lon_count):
        mirror = l - l % Y_LO + (Y_LO - 1 - l % Y_LO)
        cross.append(((split - 1) * lon_count + l, split * lon_count + mirror))
        cross.append((split * lon_count + l, (split - 1) * lon_count + mirror))
    own = lax.ppermute(piece, both, cross)
    return below, above, own


def far_side(own):
    lat_count, lon_count = lax.axis_size("lat"), lax.axis_size("lon")
    both = ("lat", "lon")
    split = lat_count // 2
    z_count = lon_count // Y_LO

    def along_z(value, shift):
        pairs = []
        for band in (split - 1, split):
            for l in range(lon_count):
                target = ((l // Y_LO + shift) % z_count) * Y_LO + l % Y_LO
                pairs.append((band * lon_count + l, band * lon_count + target))
        return lax.ppermute(value, both, pairs)

    moved = [along_z(own, 2), along_z(own, -1), along_z(own, 1)]
    return moved


def assembled(kv, own, moved):
    z = lax.axis_index("lon") // Y_LO
    quarters = jnp.stack([own, moved[1], moved[0], moved[2]])
    order = (jnp.arange(Y_LO) - z) % Y_LO
    joined = jnp.take(quarters, order, axis=0)
    return jnp.moveaxis(joined, 0, 2).reshape(kv.shape)


def gathered_rows(local, after=None):
    lon_count = lax.axis_size("lon")
    core = lax.axis_index("lat") % 2
    half = local.shape[1] // 2
    mine = lax.dynamic_slice_in_dim(local, core * half, half, axis=1)
    if after is not None:
        mine, _ = lax.optimization_barrier((mine, after))
    fetched = lax.all_to_all(jnp.tile(mine, (lon_count, 1)), "lon", 0, 0, tiled=True)
    lat_count = lax.axis_size("lat")
    swap = [(i, i ^ 1) for i in range(lat_count)]
    other = lax.ppermute(fetched, "lat", swap)
    low = jnp.where(core == 0, fetched, other)
    high = jnp.where(core == 0, other, fetched)
    return jnp.concatenate([low, high], axis=1)


def layer(queries, gain, w_query, w_out, kv_cache, nbr_lists, counts):
    rows = queries.astype(jnp.float32)
    rowwise_scale = lax.rsqrt(jnp.mean(rows * rows, axis=1, keepdims=True) + 1e-05)
    normed = (rows * rowwise_scale * gain.astype(jnp.float32)[None, :]).astype(jnp.bfloat16)
    blocks_here = kv_cache.shape[1]
    sent = neighbour_bands(kv_cache)
    w_query_rows = gathered_rows(w_query, after=sent[2])
    projected = jnp.dot(
        normed,
        w_query_rows,
        preferred_element_type=jnp.float32,
    )
    query = (projected * HD ** (-0.5)).astype(jnp.bfloat16)
    lat = lax.axis_index("lat")
    split = lax.axis_size("lat") // 2
    local_lists = jnp.clip(nbr_lists[0] - (lat - 1) * blocks_here, 0, 3 * blocks_here - 1)
    crossing = ((lat == split) & (local_lists < blocks_here)) | (
        (lat == split - 1) & (local_lists >= 2 * blocks_here)
    )
    slots = jnp.where(crossing, 3 * blocks_here + local_lists % blocks_here, local_lists)
    moved = far_side(sent[2])
    below, above, own = sent
    joined = assembled(kv_cache, own, moved)
    window = jnp.concatenate([below, kv_cache, above, joined], axis=1)
    attended = attend(query, window, slots, counts)
    w_out_rows = gathered_rows(w_out.T, after=query)
    decoded = lax.dot_general(
        attended,
        w_out_rows,
        (((1,), (1,)), ((), ())),
        preferred_element_type=jnp.float32,
    )
    return decoded.astype(jnp.bfloat16)


def solution(mesh):
    placed = (
        P(("lat", "lon"), None),
        P(),
        P("lon", None),
        P(None, "lon"),
        P(None, "lat", None, None),
        P(("lat", "lon"), None),
        P(("lat", "lon")),
    )
    return jax.shard_map(layer, mesh=mesh, in_specs=placed, out_specs=P(("lat", "lon"), None), check_vma=False)
```

```python
import jax
import jax.numpy as jnp
from jax import lax
from jax.experimental import pallas as pl
from jax.experimental.pallas import tpu as pltpu
from jax.sharding import PartitionSpec as P


HD = 64


def attention_kernel(slots_ref, sources_ref, count_ref, q_ref, *refs):
    nbr = slots_ref.shape[0]
    per_part = len(refs[:-1]) // 2
    sources = per_part // nbr
    out_ref = refs[-1]

    def block(part, slot):
        first = part * per_part + slot * sources
        picked = refs[first][...]
        for source in range(1, sources):
            picked = jnp.where(sources_ref[slot] == source, refs[first + source][...], picked)
        return picked

    keys = [block(0, slot) for slot in range(nbr)]
    values = [block(1, slot) for slot in range(nbr)]
    count = count_ref[0]
    width = q_ref.shape[1]
    lane = lax.broadcasted_iota(jnp.int32, (1, width), 1)
    q_all = q_ref[...]
    result = None
    for head in range(width // HD):
        in_head = (lane >= head * HD) & (lane < (head + 1) * HD)
        q_head = jnp.where(in_head, q_all, jnp.zeros_like(q_all))
        scores = []
        for slot, key in enumerate(keys):
            s = lax.dot_general(q_head, key, (((1,), (1,)), ((), ())), preferred_element_type=jnp.float32)
            scores.append(s if slot == 0 else jnp.where(slot < count, s, -jnp.inf))
        peak = scores[0].max(axis=1, keepdims=True)
        for s in scores[1:]:
            peak = jnp.maximum(peak, s.max(axis=1, keepdims=True))
        total = None
        mixed = None
        for s, value in zip(scores, values):
            expo = jnp.exp(s - peak)
            part = expo.sum(axis=1, keepdims=True)
            total = part if total is None else total + part
            term = jnp.dot(expo.astype(jnp.bfloat16), value, preferred_element_type=jnp.float32)
            mixed = term if mixed is None else mixed + term
        head_out = mixed / total
        result = head_out if result is None else jnp.where(in_head, head_out, result)
    out_ref[...] = result.astype(out_ref.dtype)


def attend(q, banks, slots, sources, count, lanes=128):
    rows, width = q.shape
    nbr = slots.shape[0]
    q_spec = pl.BlockSpec((rows, lanes), lambda h, s, src, c: (0, h))

    def kv_spec(part, slot, source):
        def index(h, s, src, c):
            used = src[slot] == source
            return (part, jnp.where(used, s[slot], 0), 0, jnp.where(used, h, 0))

        return pl.BlockSpec((None, None, rows, lanes), index)

    in_specs = [q_spec]
    operands = []
    for part in range(2):
        for slot in range(nbr):
            for source, bank in enumerate(banks):
                in_specs.append(kv_spec(part, slot, source))
                operands.append(bank)
    return pl.pallas_call(
        attention_kernel,
        grid_spec=pltpu.PrefetchScalarGridSpec(
            num_scalar_prefetch=3, grid=(width // lanes,), in_specs=in_specs, out_specs=q_spec),
        out_shape=jax.ShapeDtypeStruct((rows, width), jnp.bfloat16),
    )(slots, sources, count, q, *operands)


Y_LO = 4


def neighbour_bands(kv):
    lat_count, lon_count = lax.axis_size("lat"), lax.axis_size("lon")
    lon = lax.axis_index("lon")
    both = ("lat", "lon")
    split = lat_count // 2
    up = [(k * lon_count + l, (k + 1) * lon_count + l) for k in range(lat_count - 1) if k != split - 1 for l in range(lon_count)]
    below = lax.ppermute(kv, both, up)
    above = lax.ppermute(kv, both, [(j, i) for i, j in up])
    rows = kv.shape[2] // Y_LO
    z = lon // Y_LO
    piece = lax.dynamic_slice_in_dim(kv, (z % Y_LO) * rows, rows, axis=2)
    cross = []
    for l in range(lon_count):
        mirror = l - l % Y_LO + (Y_LO - 1 - l % Y_LO)
        cross.append(((split - 1) * lon_count + l, split * lon_count + mirror))
        cross.append((split * lon_count + l, (split - 1) * lon_count + mirror))
    own = lax.ppermute(piece, both, cross)
    return below, above, own


def far_side(own):
    lat_count, lon_count = lax.axis_size("lat"), lax.axis_size("lon")
    both = ("lat", "lon")
    split = lat_count // 2
    z_count = lon_count // Y_LO

    def along_z(value, shift):
        pairs = []
        for band in (split - 1, split):
            for l in range(lon_count):
                target = ((l // Y_LO + shift) % z_count) * Y_LO + l % Y_LO
                pairs.append((band * lon_count + l, band * lon_count + target))
        return lax.ppermute(value, both, pairs)

    moved = [along_z(own, 2), along_z(own, -1), along_z(own, 1)]
    return moved


def assembled(kv, own, moved):
    z = lax.axis_index("lon") // Y_LO
    quarters = jnp.stack([own, moved[1], moved[0], moved[2]])
    order = (jnp.arange(Y_LO) - z) % Y_LO
    joined = jnp.take(quarters, order, axis=0)
    return jnp.moveaxis(joined, 0, 2).reshape(kv.shape)


def gathered_rows(local, after=None):
    lon_count = lax.axis_size("lon")
    core = lax.axis_index("lat") % 2
    half = local.shape[1] // 2
    mine = lax.dynamic_slice_in_dim(local, core * half, half, axis=1)
    if after is not None:
        mine, _ = lax.optimization_barrier((mine, after))
    fetched = lax.all_to_all(jnp.tile(mine, (lon_count, 1)), "lon", 0, 0, tiled=True)
    lat_count = lax.axis_size("lat")
    swap = [(i, i ^ 1) for i in range(lat_count)]
    other = lax.ppermute(fetched, "lat", swap)
    low = jnp.where(core == 0, fetched, other)
    high = jnp.where(core == 0, other, fetched)
    return jnp.concatenate([low, high], axis=1)


def layer(queries, gain, w_query, w_out, kv_cache, nbr_lists, counts):
    rows = queries.astype(jnp.float32)
    rowwise_scale = lax.rsqrt(jnp.mean(rows * rows, axis=1, keepdims=True) + 1e-05)
    normed = (rows * rowwise_scale * gain.astype(jnp.float32)[None, :]).astype(jnp.bfloat16)
    blocks_here = kv_cache.shape[1]
    sent = neighbour_bands(kv_cache)
    w_query_rows = gathered_rows(w_query, after=sent[2])
    projected = jnp.dot(
        normed,
        w_query_rows,
        preferred_element_type=jnp.float32,
    )
    query = (projected * HD ** (-0.5)).astype(jnp.bfloat16)
    lat = lax.axis_index("lat")
    split = lax.axis_size("lat") // 2
    local_lists = jnp.clip(nbr_lists[0] - (lat - 1) * blocks_here, 0, 3 * blocks_here - 1)
    crossing = ((lat == split) & (local_lists < blocks_here)) | (
        (lat == split - 1) & (local_lists >= 2 * blocks_here)
    )
    slots = local_lists % blocks_here
    sources = jnp.where(crossing, 3, local_lists // blocks_here)
    moved = far_side(sent[2])
    below, above, own = sent
    joined = assembled(kv_cache, own, moved)
    attended = attend(query, (below, kv_cache, above, joined), slots, sources, counts)
    w_out_rows = gathered_rows(w_out.T, after=query)
    decoded = lax.dot_general(
        attended,
        w_out_rows,
        (((1,), (1,)), ((), ())),
        preferred_element_type=jnp.float32,
    )
    return decoded.astype(jnp.bfloat16)


def solution(mesh):
    placed = (
        P(("lat", "lon"), None),
        P(),
        P("lon", None),
        P(None, "lon"),
        P(None, "lat", None, None),
        P(("lat", "lon"), None),
        P(("lat", "lon")),
    )
    return jax.shard_map(
        layer, mesh=mesh, in_specs=placed, out_specs=P(("lat", "lon"), None), check_vma=False
    )
```

```python
import jax
import jax.numpy as jnp
from jax import lax
from jax.experimental import pallas as pl
from jax.experimental.pallas import tpu as pltpu
from jax.sharding import PartitionSpec as P


HD = 64


def attention_kernel(slots_ref, count_ref, q_ref, *refs):
    key_refs, value_refs, out_ref = refs[: (len(refs) - 1) // 2], refs[(len(refs) - 1) // 2 : -1], refs[-1]
    count = count_ref[0]
    width = q_ref.shape[1]
    lane = lax.broadcasted_iota(jnp.int32, (1, width), 1)
    q_all = q_ref[...]
    result = None
    for head in range(width // HD):
        in_head = (lane >= head * HD) & (lane < (head + 1) * HD)
        q_head = jnp.where(in_head, q_all, jnp.zeros_like(q_all))
        scores = []
        for slot, key_ref in enumerate(key_refs):
            s = lax.dot_general(q_head, key_ref[...], (((1,), (1,)), ((), ())), preferred_element_type=jnp.float32)
            scores.append(jnp.where(slot < count, s, -jnp.inf))
        peak = scores[0].max(axis=1, keepdims=True)
        for s in scores[1:]:
            peak = jnp.maximum(peak, s.max(axis=1, keepdims=True))
        total = None
        mixed = None
        for s, value_ref in zip(scores, value_refs):
            expo = jnp.exp(s - peak)
            part = expo.sum(axis=1, keepdims=True)
            total = part if total is None else total + part
            term = jnp.dot(expo.astype(jnp.bfloat16), value_ref[...], preferred_element_type=jnp.float32)
            mixed = term if mixed is None else mixed + term
        head_out = mixed / total
        result = head_out if result is None else jnp.where(in_head, head_out, result)
    out_ref[...] = result.astype(out_ref.dtype)


def attend(q, window, slots, count, lanes=128):
    rows, width = q.shape
    nbr = slots.shape[0]
    q_spec = pl.BlockSpec((rows, lanes), lambda h, s, c: (0, h))

    def kv_spec(part, slot):
        return pl.BlockSpec((None, None, rows, lanes), lambda h, s, c: (part, s[slot], 0, h))

    in_specs = [q_spec] + [kv_spec(0, j) for j in range(nbr)] + [kv_spec(1, j) for j in range(nbr)]
    return pl.pallas_call(
        attention_kernel,
        grid_spec=pltpu.PrefetchScalarGridSpec(
            num_scalar_prefetch=2, grid=(width // lanes,), in_specs=in_specs, out_specs=q_spec),
        out_shape=jax.ShapeDtypeStruct((rows, width), jnp.bfloat16),
    )(slots, count, q, *([window] * (2 * nbr)))


Y_LO = 4


def neighbour_bands(kv):
    lat_count, lon_count = lax.axis_size("lat"), lax.axis_size("lon")
    lon = lax.axis_index("lon")
    both = ("lat", "lon")
    split = lat_count // 2
    up = [(k * lon_count + l, (k + 1) * lon_count + l) for k in range(lat_count - 1) if k != split - 1 for l in range(lon_count)]
    below = lax.ppermute(kv, both, up)
    above = lax.ppermute(kv, both, [(j, i) for i, j in up])
    rows = kv.shape[2] // Y_LO
    z = lon // Y_LO
    piece = lax.dynamic_slice_in_dim(kv, (z % Y_LO) * rows, rows, axis=2)
    cross = []
    for l in range(lon_count):
        mirror = l - l % Y_LO + (Y_LO - 1 - l % Y_LO)
        cross.append(((split - 1) * lon_count + l, split * lon_count + mirror))
        cross.append((split * lon_count + l, (split - 1) * lon_count + mirror))
    own = lax.ppermute(piece, both, cross)
    return below, above, own


def far_side(own):
    lat_count, lon_count = lax.axis_size("lat"), lax.axis_size("lon")
    both = ("lat", "lon")
    split = lat_count // 2
    z_count = lon_count // Y_LO

    def along_z(value, shift):
        pairs = []
        for band in (split - 1, split):
            for l in range(lon_count):
                target = ((l // Y_LO + shift) % z_count) * Y_LO + l % Y_LO
                pairs.append((band * lon_count + l, band * lon_count + target))
        return lax.ppermute(value, both, pairs)

    moved = [along_z(own, 2), along_z(own, -1), along_z(own, 1)]
    return moved


def assembled(kv, below, above, own, moved):
    lat_count = lax.axis_size("lat")
    lat, lon = lax.axis_index("lat"), lax.axis_index("lon")
    split = lat_count // 2
    z = lon // Y_LO
    quarters = jnp.stack([own, moved[1], moved[0], moved[2]])
    order = (jnp.arange(Y_LO) - z) % Y_LO
    joined = jnp.take(quarters, order, axis=0)
    joined = jnp.moveaxis(joined, 0, 2).reshape(kv.shape)
    below = jnp.where(lat == split, joined, below)
    above = jnp.where(lat == split - 1, joined, above)
    return below, above


def gathered_rows(local, after=None):
    lon_count = lax.axis_size("lon")
    core = lax.axis_index("lat") % 2
    half = local.shape[1] // 2
    mine = lax.dynamic_slice_in_dim(local, core * half, half, axis=1)
    if after is not None:
        mine, _ = lax.optimization_barrier((mine, after))
    fetched = lax.all_to_all(jnp.tile(mine, (lon_count, 1)), "lon", 0, 0, tiled=True)
    lat_count = lax.axis_size("lat")
    swap = [(i, i ^ 1) for i in range(lat_count)]
    other = lax.ppermute(fetched, "lat", swap)
    return fetched, other


def layer(queries, gain, w_query, w_out, kv_cache, nbr_lists, counts):
    rows = queries.astype(jnp.float32)
    rowwise_scale = lax.rsqrt(jnp.mean(rows * rows, axis=1, keepdims=True) + 1e-05)
    normed = (rows * rowwise_scale * gain.astype(jnp.float32)[None, :]).astype(jnp.bfloat16)
    blocks_here = kv_cache.shape[1]
    sent = neighbour_bands(kv_cache)
    w_query_rows = gathered_rows(w_query, after=sent[2])
    core = lax.axis_index("lat") % 2
    mine, theirs = (
        (jnp.dot(normed, half, preferred_element_type=jnp.float32) * HD ** (-0.5)).astype(jnp.bfloat16)
        for half in w_query_rows
    )
    query = jnp.where(core == 0, jnp.concatenate([mine, theirs], axis=1), jnp.concatenate([theirs, mine], axis=1))
    local_lists = nbr_lists - (lax.axis_index("lat") - 1) * blocks_here
    slots = jnp.clip(local_lists[0], 0, 3 * blocks_here - 1)
    moved = far_side(sent[2])
    below, above = assembled(kv_cache, *sent, moved)
    window = jnp.concatenate([below, kv_cache, above], axis=1)
    attended = attend(query, window, slots, counts)
    w_out_rows = gathered_rows(w_out.T, after=query)
    half = attended.shape[1] // 2
    own_half = lax.dynamic_slice_in_dim(attended, core * half, half, axis=1)
    other_half = lax.dynamic_slice_in_dim(attended, (1 - core) * half, half, axis=1)
    contract = (((1,), (1,)), ((), ()))
    decoded = lax.dot_general(own_half, w_out_rows[0], contract, preferred_element_type=jnp.float32)
    decoded = decoded + lax.dot_general(other_half, w_out_rows[1], contract, preferred_element_type=jnp.float32)
    return decoded.astype(jnp.bfloat16)


def solution(mesh):
    placed = (
        P(("lat", "lon"), None),
        P(),
        P("lon", None),
        P(None, "lon"),
        P(None, "lat", None, None),
        P(("lat", "lon"), None),
        P(("lat", "lon")),
    )
    return jax.shard_map(layer, mesh=mesh, in_specs=placed, out_specs=P(("lat", "lon"), None), check_vma=False)
```

```python
import jax
import jax.numpy as jnp
from jax import lax
from jax.experimental import pallas as pl
from jax.experimental.pallas import tpu as pltpu
from jax.sharding import PartitionSpec as P


HD = 64


def attention_kernel(slots_ref, count_ref, q_ref, *refs):
    key_refs, value_refs, out_ref = refs[: (len(refs) - 1) // 2], refs[(len(refs) - 1) // 2 : -1], refs[-1]
    count = count_ref[0]
    width = q_ref.shape[1]
    lane = lax.broadcasted_iota(jnp.int32, (1, width), 1)
    q_all = q_ref[...]
    result = None
    for head in range(width // HD):
        in_head = (lane >= head * HD) & (lane < (head + 1) * HD)
        q_head = jnp.where(in_head, q_all, jnp.zeros_like(q_all))
        scores = []
        for slot, key_ref in enumerate(key_refs):
            s = lax.dot_general(q_head, key_ref[...], (((1,), (1,)), ((), ())), preferred_element_type=jnp.float32)
            scores.append(s if slot == 0 else jnp.where(slot < count, s, -jnp.inf))
        peak = scores[0].max(axis=1, keepdims=True)
        for s in scores[1:]:
            peak = jnp.maximum(peak, s.max(axis=1, keepdims=True))
        total = None
        mixed = None
        for s, value_ref in zip(scores, value_refs):
            expo = jnp.exp(s - peak)
            part = expo.sum(axis=1, keepdims=True)
            total = part if total is None else total + part
            term = jnp.dot(expo.astype(jnp.bfloat16), value_ref[...], preferred_element_type=jnp.float32)
            mixed = term if mixed is None else mixed + term
        head_out = mixed / total
        result = head_out if result is None else jnp.where(in_head, head_out, result)
    out_ref[...] = result.astype(out_ref.dtype)


def attend(q, window, slots, count, lanes=256):
    rows, width = q.shape
    nbr = slots.shape[0]
    q_spec = pl.BlockSpec((rows, lanes), lambda h, s, c: (0, h))

    def kv_spec(part, slot):
        return pl.BlockSpec((None, None, rows, lanes), lambda h, s, c: (part, s[slot], 0, h))

    in_specs = [q_spec] + [kv_spec(0, j) for j in range(nbr)] + [kv_spec(1, j) for j in range(nbr)]
    return pl.pallas_call(
        attention_kernel,
        grid_spec=pltpu.PrefetchScalarGridSpec(
            num_scalar_prefetch=2, grid=(width // lanes,), in_specs=in_specs, out_specs=q_spec),
        out_shape=jax.ShapeDtypeStruct((rows, width), jnp.bfloat16),
    )(slots, count, q, *([window] * (2 * nbr)))


Y_LO = 4


def neighbour_bands(kv):
    lat_count, lon_count = lax.axis_size("lat"), lax.axis_size("lon")
    lon = lax.axis_index("lon")
    both = ("lat", "lon")
    split = lat_count // 2
    up = [(k * lon_count + l, (k + 1) * lon_count + l) for k in range(lat_count - 1) if k != split - 1 for l in range(lon_count)]
    below = lax.ppermute(kv, both, up)
    above = lax.ppermute(kv, both, [(j, i) for i, j in up])
    rows = kv.shape[2] // Y_LO
    z = lon // Y_LO
    piece = lax.dynamic_slice_in_dim(kv, (z % Y_LO) * rows, rows, axis=2)
    cross = []
    for l in range(lon_count):
        mirror = l - l % Y_LO + (Y_LO - 1 - l % Y_LO)
        cross.append(((split - 1) * lon_count + l, split * lon_count + mirror))
        cross.append((split * lon_count + l, (split - 1) * lon_count + mirror))
    own = lax.ppermute(piece, both, cross)
    return below, above, own


def far_side(own):
    lat_count, lon_count = lax.axis_size("lat"), lax.axis_size("lon")
    both = ("lat", "lon")
    split = lat_count // 2
    z_count = lon_count // Y_LO

    def along_z(value, shift):
        pairs = []
        for band in (split - 1, split):
            for l in range(lon_count):
                target = ((l // Y_LO + shift) % z_count) * Y_LO + l % Y_LO
                pairs.append((band * lon_count + l, band * lon_count + target))
        return lax.ppermute(value, both, pairs)

    moved = [along_z(own, 2), along_z(own, -1), along_z(own, 1)]
    return moved


def assembled(kv, below, above, own, moved):
    lat_count = lax.axis_size("lat")
    lat, lon = lax.axis_index("lat"), lax.axis_index("lon")
    split = lat_count // 2
    z = lon // Y_LO
    quarters = jnp.stack([own, moved[1], moved[0], moved[2]])
    order = (jnp.arange(Y_LO) - z) % Y_LO
    joined = jnp.take(quarters, order, axis=0)
    joined = jnp.moveaxis(joined, 0, 2).reshape(kv.shape)
    below = jnp.where(lat == split, joined, below)
    above = jnp.where(lat == split - 1, joined, above)
    return below, above


def gathered_rows(local, after=None):
    lon_count = lax.axis_size("lon")
    core = lax.axis_index("lat") % 2
    half = local.shape[1] // 2
    mine = lax.dynamic_slice_in_dim(local, core * half, half, axis=1)
    if after is not None:
        mine, _ = lax.optimization_barrier((mine, after))
    fetched = lax.all_to_all(jnp.tile(mine, (lon_count, 1)), "lon", 0, 0, tiled=True)
    lat_count = lax.axis_size("lat")
    swap = [(i, i ^ 1) for i in range(lat_count)]
    other = lax.ppermute(fetched, "lat", swap)
    low = jnp.where(core == 0, fetched, other)
    high = jnp.where(core == 0, other, fetched)
    return jnp.concatenate([low, high], axis=1)


def layer(queries, gain, w_query, w_out, kv_cache, nbr_lists, counts):
    rows = queries.astype(jnp.float32)
    rowwise_scale = lax.rsqrt(jnp.mean(rows * rows, axis=1, keepdims=True) + 1e-05)
    normed = (rows * rowwise_scale * gain.astype(jnp.float32)[None, :]).astype(jnp.bfloat16)
    blocks_here = kv_cache.shape[1]
    sent = neighbour_bands(kv_cache)
    w_query_rows = gathered_rows(w_query, after=sent[2])
    projected = jnp.dot(
        normed,
        w_query_rows,
        preferred_element_type=jnp.float32,
    )
    query = (projected * HD ** (-0.5)).astype(jnp.bfloat16)
    local_lists = nbr_lists - (lax.axis_index("lat") - 1) * blocks_here
    slots = jnp.clip(local_lists[0], 0, 3 * blocks_here - 1)
    moved = far_side(sent[2])
    below, above = assembled(kv_cache, *sent, moved)
    window = jnp.concatenate([below, kv_cache, above], axis=1)
    attended = attend(query, window, slots, counts)
    w_out_rows = gathered_rows(w_out.T, after=query)
    decoded = lax.dot_general(
        attended,
        w_out_rows,
        (((1,), (1,)), ((), ())),
        preferred_element_type=jnp.float32,
    )
    return decoded.astype(jnp.bfloat16)


def solution(mesh):
    placed = (
        P(("lat", "lon"), None),
        P(),
        P("lon", None),
        P(None, "lon"),
        P(None, "lat", None, None),
        P(("lat", "lon"), None),
        P(("lat", "lon")),
    )
    return jax.shard_map(layer, mesh=mesh, in_specs=placed, out_specs=P(("lat", "lon"), None), check_vma=False)
```

```python
import jax
import jax.numpy as jnp
from jax import lax
from jax.experimental import pallas as pl
from jax.experimental.pallas import tpu as pltpu
from jax.sharding import PartitionSpec as P


HD = 64


def attention_kernel(slots_ref, count_ref, q_ref, *refs):
    key_refs, value_refs, out_ref = refs[: (len(refs) - 1) // 2], refs[(len(refs) - 1) // 2 : -1], refs[-1]
    count = count_ref[0]
    width = q_ref.shape[1]
    lane = lax.broadcasted_iota(jnp.int32, (1, width), 1)
    q_all = q_ref[...]
    result = None
    for head in range(width // HD):
        in_head = (lane >= head * HD) & (lane < (head + 1) * HD)
        q_head = jnp.where(in_head, q_all, jnp.zeros_like(q_all))
        scores = []
        for slot, key_ref in enumerate(key_refs):
            s = lax.dot_general(q_head, key_ref[...], (((1,), (1,)), ((), ())), preferred_element_type=jnp.float32)
            scores.append(jnp.where(slot < count, s, -jnp.inf))
        peak = scores[0].max(axis=1, keepdims=True)
        for s in scores[1:]:
            peak = jnp.maximum(peak, s.max(axis=1, keepdims=True))
        total = None
        mixed = None
        for s, value_ref in zip(scores, value_refs):
            expo = jnp.exp(s - peak)
            part = expo.sum(axis=1, keepdims=True)
            total = part if total is None else total + part
            term = jnp.dot(expo.astype(jnp.bfloat16), value_ref[...], preferred_element_type=jnp.float32)
            mixed = term if mixed is None else mixed + term
        head_out = mixed / total
        result = head_out if result is None else jnp.where(in_head, head_out, result)
    out_ref[...] = result.astype(out_ref.dtype)


def attend(q, window, slots, count, lanes=256):
    rows, width = q.shape
    nbr = slots.shape[0]
    q_spec = pl.BlockSpec((rows, lanes), lambda h, s, c: (0, h))

    def kv_spec(part, slot):
        return pl.BlockSpec((None, None, rows, lanes), lambda h, s, c: (part, s[slot], 0, h))

    in_specs = [q_spec] + [kv_spec(0, j) for j in range(nbr)] + [kv_spec(1, j) for j in range(nbr)]
    return pl.pallas_call(
        attention_kernel,
        grid_spec=pltpu.PrefetchScalarGridSpec(
            num_scalar_prefetch=2, grid=(width // lanes,), in_specs=in_specs, out_specs=q_spec),
        out_shape=jax.ShapeDtypeStruct((rows, width), jnp.bfloat16),
    )(slots, count, q, *([window] * (2 * nbr)))


Y_LO = 4


def neighbour_bands(kv):
    lat_count, lon_count = lax.axis_size("lat"), lax.axis_size("lon")
    lon = lax.axis_index("lon")
    both = ("lat", "lon")
    split = lat_count // 2
    up = [(k * lon_count + l, (k + 1) * lon_count + l) for k in range(lat_count - 1) if k != split - 1 for l in range(lon_count)]
    below = lax.ppermute(kv, both, up)
    above = lax.ppermute(kv, both, [(j, i) for i, j in up])
    rows = kv.shape[2] // Y_LO
    z = lon // Y_LO
    piece = lax.dynamic_slice_in_dim(kv, (z % Y_LO) * rows, rows, axis=2)
    cross = []
    for l in range(lon_count):
        mirror = l - l % Y_LO + (Y_LO - 1 - l % Y_LO)
        cross.append(((split - 1) * lon_count + l, split * lon_count + mirror))
        cross.append((split * lon_count + l, (split - 1) * lon_count + mirror))
    own = lax.ppermute(piece, both, cross)
    return below, above, own


def far_side(own):
    lat_count, lon_count = lax.axis_size("lat"), lax.axis_size("lon")
    both = ("lat", "lon")
    split = lat_count // 2
    z_count = lon_count // Y_LO

    def along_z(value, shift):
        pairs = []
        for band in (split - 1, split):
            for l in range(lon_count):
                target = ((l // Y_LO + shift) % z_count) * Y_LO + l % Y_LO
                pairs.append((band * lon_count + l, band * lon_count + target))
        return lax.ppermute(value, both, pairs)

    moved = [along_z(own, 2), along_z(own, -1), along_z(own, 1)]
    return moved


def assembled(below, above, own, moved):
    lat_count = lax.axis_size("lat")
    lat, lon = lax.axis_index("lat"), lax.axis_index("lon")
    split = lat_count // 2
    z = lon // Y_LO
    joined = jnp.roll(jnp.concatenate([own, moved[1], moved[0], moved[2]], axis=2), z * own.shape[2], axis=2)
    below = jnp.where(lat == split, joined, below)
    above = jnp.where(lat == split - 1, joined, above)
    return below, above


def gathered_rows(local, after=None):
    lon_count = lax.axis_size("lon")
    core = lax.axis_index("lat") % 2
    half = local.shape[1] // 2
    mine = lax.dynamic_slice_in_dim(local, core * half, half, axis=1)
    if after is not None:
        mine, _ = lax.optimization_barrier((mine, after))
    fetched = lax.all_to_all(jnp.tile(mine, (lon_count, 1)), "lon", 0, 0, tiled=True)
    lat_count = lax.axis_size("lat")
    swap = [(i, i ^ 1) for i in range(lat_count)]
    other = lax.ppermute(fetched, "lat", swap)
    low = jnp.where(core == 0, fetched, other)
    high = jnp.where(core == 0, other, fetched)
    return jnp.concatenate([low, high], axis=1)


def layer(queries, gain, w_query, w_out, kv_cache, nbr_lists, counts):
    rows = queries.astype(jnp.float32)
    rowwise_scale = lax.rsqrt(jnp.mean(rows * rows, axis=1, keepdims=True) + 1e-05)
    normed = (rows * rowwise_scale * gain.astype(jnp.float32)[None, :]).astype(jnp.bfloat16)
    blocks_here = kv_cache.shape[1]
    sent = neighbour_bands(kv_cache)
    w_query_rows = gathered_rows(w_query, after=sent[2])
    projected = jnp.dot(
        normed,
        w_query_rows,
        preferred_element_type=jnp.float32,
    )
    query = (projected * HD ** (-0.5)).astype(jnp.bfloat16)
    local_lists = nbr_lists - (lax.axis_index("lat") - 1) * blocks_here
    slots = jnp.clip(local_lists[0], 0, 3 * blocks_here - 1)
    moved = far_side(sent[2])
    below, above = assembled(*sent, moved)
    window = jnp.concatenate([below, kv_cache, above], axis=1)
    attended = attend(query, window, slots, counts)
    w_out_rows = gathered_rows(w_out.T, after=query)
    decoded = lax.dot_general(
        attended,
        w_out_rows,
        (((1,), (1,)), ((), ())),
        preferred_element_type=jnp.float32,
    )
    return decoded.astype(jnp.bfloat16)


def solution(mesh):
    placed = (
        P(("lat", "lon"), None),
        P(),
        P("lon", None),
        P(None, "lon"),
        P(None, "lat", None, None),
        P(("lat", "lon"), None),
        P(("lat", "lon")),
    )
    return jax.shard_map(layer, mesh=mesh, in_specs=placed, out_specs=P(("lat", "lon"), None), check_vma=False)
```
